256 devices in a mesh: seq: 32 (over y, z), chan: 8 (over x, core).
Axes of the slice: x: 4, y: 4, z: 8, core: 2. Of those that a mesh axis runs over, the one named last changes fastest.
Arguments:
- loaded: bfloat16 [3, 32768, 4096], P(None, 'seq', 'chan'), may hold values from -6 to 6
- counts: int32 [32], P('seq'), may hold values from 0 to 1024, as said below
- short_taps: float32 [3, 3, 4096], P(None, None, 'chan'), may hold values from -3 to 3
- filters: float32 [16384, 4096], P('seq', 'chan'), may hold values from -0.046875 to 0.046875
- skip_gain: float32 [4096], P('chan'), may hold values from 0.5 to 1.5
- out_weight: bfloat16 [4096, 4096], P('chan'), may hold values from -0.09375 to 0.09375
Outputs:
- mixed_t: bfloat16 [4096, 16384], P('chan', 'seq')
The draws below stay inside these ranges and needn't reach their ends.
Inputs may be any that keep to these rules, and one draw needn't show every extreme that they name: `counts`: the buffers of indices 2k and 2k + 1 of seq together hold exactly 1024 live rows.
All inputs are finite; a program needn't handle non-finite values.
Results may differ from the reference program's by a relative error of at most 0.005.
Values may be sent and summed in bfloat16 or wider, within the bound.
No kernel may reach another device: no remote copies, remote signals or barrier semaphores. Data moves between devices by JAX's collectives and lax.ppermute only.
A program may use at most 128 MiB of HBM per device.

```python
import math
import jax
import jax.numpy as jnp
from jax import lax

D = 4096
B = 512
L = 16384
N_SEQ = 32


def draw_counts(key, part):
    pair_count = N_SEQ // 2
    first = jax.random.randint(jax.random.fold_in(key, 11), (pair_count,), 1, 2 * B)
    forced = jax.random.randint(jax.random.fold_in(key, 12), (), 0, pair_count)
    first = jnp.where(jnp.arange(pair_count) == forced, 2 * B, first)
    return jnp.stack([first, 2 * B - first], axis=-1).reshape(N_SEQ).astype(jnp.int32)


def level_of(key, shape, shards, smallest, top_value):
    level, own = 1.0, jax.random.fold_in(key, 6)
    for dim, blocks in shards:
        steps = jnp.exp(jax.random.uniform(jax.random.fold_in(own, dim), (blocks,), jnp.float32, smallest / len(shards), top_value / len(shards)))
        level = level * jnp.repeat(steps, shape[dim] // blocks).reshape([-1 if axis == dim else 1 for axis in range(len(shape))])
    return level


def noise(stream_key, shape, scale, most, split=(), kind=jnp.bfloat16):
    gain = level_of(stream_key, shape, split, -0.22, 0.18) if split else 1.0
    array = jax.random.normal(stream_key, shape, jnp.float32) * scale * gain
    return jnp.minimum(jnp.maximum(array, -most), most).astype(kind)


def setup_inputs(seed: int = 0) -> dict:
    seeds = jax.random.split(jax.random.key(seed), 7)
    loaded = noise(seeds[0], (3, 2 * B * N_SEQ, D), 1.0, 6.0, ((1, 32), (2, 8)))
    counts = draw_counts(jax.random.fold_in(seeds[6], 71), 0)
    short_taps = noise(seeds[2], (3, 3, D), 0.5, 3.0, ((2, 8),), jnp.float32)
    filters = noise(seeds[3], (L, D), L ** -0.5, 0.046875, ((0, 32), (1, 8)), jnp.float32)
    skip_gain = jnp.clip(0.5 + 1.0 * jax.random.uniform(seeds[4], (D,), jnp.float32) ** level_of(seeds[4], (D,), ((0, 8),), -0.2, 0.2), 0.5, 1.5)
    out_weight = noise(seeds[5], (D, D), D ** -0.5, 0.09375, ((0, 8),))
    return {"loaded": loaded, "counts": counts, "short_taps": short_taps, "filters": filters, "skip_gain": skip_gain, "out_weight": out_weight}


def reference(loaded, counts, short_taps, filters, skip_gain, out_weight):
    seq_len = B * N_SEQ
    offsets = jnp.cumsum(counts) - counts
    slot_ids = jnp.arange(2 * B, dtype=jnp.int32)
    targets = offsets[:, None] + slot_ids[None, :]
    valid = slot_ids[None, :] < counts[:, None]
    targets = jnp.where(valid, targets, seq_len).reshape(-1).astype(jnp.int32)
    packed = jnp.zeros((3, seq_len + 1, D), jnp.bfloat16).at[:, targets, :].set(loaded)[:, :seq_len]
    block_width = math.gcd(D, 512)
    blocks = D // block_width
    packed_blocks = jnp.moveaxis(packed.reshape(3, seq_len, blocks, block_width), 2, 0)
    tap_blocks = jnp.moveaxis(short_taps.reshape(3, 3, blocks, block_width), 2, 0)
    filter_blocks = jnp.moveaxis(filters.reshape(seq_len, blocks, block_width), 1, 0)
    gain_blocks = skip_gain.reshape(blocks, block_width)

    def one_block(inputs):
        streams, taps, lags, gains = inputs
        values = streams.astype(jnp.float32)
        padded = jnp.pad(values, ((0, 0), (2, 0), (0, 0)))
        filtered = sum(taps[tap_index][:, None, :] * padded[:, 2 - tap_index:2 - tap_index + seq_len] for tap_index in range(3))
        signal = filtered[0] * filtered[1]
        spec_signal = jnp.fft.rfft(signal, 2 * seq_len, axis=0)
        spec_filter = jnp.fft.rfft(lags, 2 * seq_len, axis=0)
        conv = jnp.fft.irfft(spec_signal * spec_filter, 2 * seq_len, axis=0)[:seq_len]
        return (filtered[2] * (conv + gains[None, :] * signal)).astype(jnp.bfloat16)

    gated_blocks = lax.map(one_block, (packed_blocks, tap_blocks, filter_blocks, gain_blocks))
    gated = jnp.moveaxis(gated_blocks, 0, 1).reshape(seq_len, D)
    mixed = jnp.dot(gated, out_weight, preferred_element_type=jnp.float32).astype(jnp.bfloat16)
    return mixed.T
```

```python
import math

import jax
import jax.numpy as jnp
from jax import lax
from jax.sharding import PartitionSpec as P

highest = lax.Precision.HIGHEST


def from_partner(value, axis, distance):
    mask = 2**distance
    pairs = [(source, source ^ mask) for source in range(lax.axis_size(axis))]
    return lax.ppermute(value, axis, pairs)


def shifted(block, axis, distance):
    devices = range(lax.axis_size(axis))
    route = [(i - distance, i) for i in devices if i - distance in devices]
    return lax.ppermute(block, axis, route)


def phase_table(out_ids, in_ids, modulus):
    product = out_ids[:, None] * in_ids[None, :] % modulus
    angle = product.astype(jnp.float32) * (2.0 * math.pi / modulus)
    return (jnp.cos(angle), jnp.sin(angle))


def channel_conv(signal, filters, seq_count):
    block_rows = signal.shape[0]
    stacked = jnp.stack([signal, filters]).astype(jnp.bfloat16)
    whole = lax.all_to_all(stacked, "seq", split_axis=2, concat_axis=1, tiled=True)
    whole = whole.astype(jnp.float32)
    seq_len = whole.shape[1]
    narrow = whole.shape[2]
    outer = 2 * seq_count
    modulus = block_rows * outer
    padded = jnp.concatenate([whole, jnp.zeros_like(whole)], axis=1)
    grid = padded.reshape(2, block_rows, outer, narrow)
    inner_ids = jnp.arange(block_rows, dtype=jnp.int32)
    outer_ids = jnp.arange(outer, dtype=jnp.int32)
    cos_in, sin_in = phase_table(inner_ids, inner_ids, block_rows)
    cos_out, sin_out = phase_table(outer_ids, outer_ids, outer)
    cos_tw, sin_tw = phase_table(inner_ids, outer_ids, modulus)
    part_re = jnp.einsum("kn,snpc->skpc", cos_in, grid, precision=highest)
    part_im = -jnp.einsum("kn,snpc->skpc", sin_in, grid, precision=highest)
    twist_re = part_re * cos_tw[None, :, :, None] + part_im * sin_tw[None, :, :, None]
    twist_im = part_im * cos_tw[None, :, :, None] - part_re * sin_tw[None, :, :, None]
    spec_re = jnp.einsum("kp,sqpc->sqkc", cos_out, twist_re, precision=highest) + jnp.einsum(
        "kp,sqpc->sqkc", sin_out, twist_im, precision=highest
    )
    spec_im = jnp.einsum("kp,sqpc->sqkc", cos_out, twist_im, precision=highest) - jnp.einsum(
        "kp,sqpc->sqkc", sin_out, twist_re, precision=highest
    )
    prod_re = spec_re[0] * spec_re[1] - spec_im[0] * spec_im[1]
    prod_im = spec_re[0] * spec_im[1] + spec_im[0] * spec_re[1]
    back_re = jnp.einsum("nk,qkc->qnc", cos_out, prod_re, precision=highest) - jnp.einsum(
        "nk,qkc->qnc", sin_out, prod_im, precision=highest
    )
    back_im = jnp.einsum("nk,qkc->qnc", cos_out, prod_im, precision=highest) + jnp.einsum(
        "nk,qkc->qnc", sin_out, prod_re, precision=highest
    )
    turn_re = back_re * cos_tw[:, :, None] - back_im * sin_tw[:, :, None]
    turn_im = back_im * cos_tw[:, :, None] + back_re * sin_tw[:, :, None]
    series = jnp.einsum("nk,kpc->npc", cos_in, turn_re, precision=highest) - jnp.einsum(
        "nk,kpc->npc", sin_in, turn_im, precision=highest
    )
    series = series.reshape(modulus, narrow)[:seq_len] / modulus
    return lax.all_to_all(series, "seq", split_axis=0, concat_axis=1, tiled=True)


def on_device(loaded, counts, short_taps, filters, skip_gain, out_weight):
    seq_count = lax.axis_size("seq")
    my_index = lax.axis_index("seq")
    block_rows = filters.shape[0]
    parity = my_index % 2
    mate_count = from_partner(counts, "seq", 0)
    first_count = jnp.where(parity == 0, counts[0], mate_count[0])
    send_start = block_rows * (1 - parity)
    half = lax.dynamic_slice_in_dim(loaded, send_start, block_rows, 1)
    recv = from_partner(half, "seq", 0)
    first = jnp.where(parity == 0, loaded[:, :block_rows], recv)
    zeros = jnp.zeros_like(recv)
    second_src = jnp.where(
        parity == 0,
        jnp.concatenate([zeros, zeros, recv], axis=1),
        jnp.concatenate([zeros, loaded], axis=1),
    )
    second = lax.dynamic_slice_in_dim(second_src, 2 * block_rows - first_count, block_rows, 1)
    rows = jnp.arange(block_rows, dtype=jnp.int32)
    use_first = rows < first_count - block_rows * parity
    packed = jnp.where(use_first[None, :, None], first, second)
    rim_rows = shifted(packed[:, block_rows - 2 :], "seq", 1)
    extended = jnp.concatenate([rim_rows, packed], axis=1).astype(jnp.float32)
    filtered = sum(
        (
            short_taps[tap_index][:, None, :]
            * extended[:, 2 - tap_index : 2 - tap_index + block_rows]
            for tap_index in range(3)
        )
    )
    signal = filtered[0] * filtered[1]
    conv = channel_conv(signal, filters, seq_count)
    gated = (filtered[2] * (conv + skip_gain[None, :] * signal)).astype(jnp.bfloat16)
    mixed = lax.psum_scatter(
        lax.dot_general(
            out_weight, gated, (((0,), (1,)), ((), ())), preferred_element_type=jnp.float32
        ),
        "chan",
        scatter_dimension=0,
        tiled=True,
    )
    return mixed.astype(jnp.bfloat16)


def solution(mesh):
    placed = (
        P(None, "seq", "chan"),
        P("seq"),
        P(None, None, "chan"),
        P("seq", "chan"),
        P("chan"),
        P("chan", None),
    )
    return jax.shard_map(
        on_device, mesh=mesh, in_specs=placed, out_specs=P("chan", "seq"), check_vma=False
    )
```

```python
import functools
import math

import jax
import jax.numpy as jnp
from jax import lax
from jax.sharding import PartitionSpec as P


def from_partner(value, axis, distance):
    mask = 2**distance
    pairs = [(source, source ^ mask) for source in range(lax.axis_size(axis))]
    return lax.ppermute(value, axis, pairs)


def shifted(block, axis, distance):
    devices = range(lax.axis_size(axis))
    route = [(i - distance, i) for i in devices if i - distance in devices]
    return lax.ppermute(block, axis, route)


def phase_table(out_ids, in_ids, modulus):
    product = out_ids[:, None] * in_ids[None, :] % modulus
    angle = product.astype(jnp.float32) * (2.0 * math.pi / modulus)
    return (jnp.cos(angle), jnp.sin(angle))


def channel_conv(signal, filters):
    stacked = jnp.swapaxes(jnp.stack([signal, filters]).astype(jnp.bfloat16), 1, 2)
    whole = lax.all_to_all(stacked, "seq", split_axis=1, concat_axis=2, tiled=True)
    streams, narrow, seq_len = whole.shape
    size = 2 * seq_len
    outer = 256
    inner = size // outer
    rows = seq_len // inner
    grid = whole.astype(jnp.float32).reshape(streams, narrow, rows, inner)
    outer_ids = jnp.arange(outer, dtype=jnp.int32)
    inner_ids = jnp.arange(inner, dtype=jnp.int32)
    cos_out, sin_out = phase_table(outer_ids, outer_ids[:rows], outer)
    cos_tw, sin_tw = phase_table(outer_ids, inner_ids, size)
    cos_in, sin_in = phase_table(inner_ids, inner_ids, inner)
    dot = functools.partial(jnp.einsum, precision=lax.Precision.HIGH)
    part_re = dot("kn,scnm->sckm", cos_out, grid)
    part_im = -dot("kn,scnm->sckm", sin_out, grid)
    twist_re = part_re * cos_tw + part_im * sin_tw
    twist_im = part_im * cos_tw - part_re * sin_tw
    spec_re = dot("sckm,mq->sckq", twist_re, cos_in) + dot("sckm,mq->sckq", twist_im, sin_in)
    spec_im = dot("sckm,mq->sckq", twist_im, cos_in) - dot("sckm,mq->sckq", twist_re, sin_in)
    prod_re = spec_re[0] * spec_re[1] - spec_im[0] * spec_im[1]
    prod_im = spec_re[0] * spec_im[1] + spec_im[0] * spec_re[1]
    back_re = dot("ckq,qm->ckm", prod_re, cos_in) - dot("ckq,qm->ckm", prod_im, sin_in)
    back_im = dot("ckq,qm->ckm", prod_im, cos_in) + dot("ckq,qm->ckm", prod_re, sin_in)
    turn_re = back_re * cos_tw - back_im * sin_tw
    turn_im = back_im * cos_tw + back_re * sin_tw
    series = dot("kn,ckm->cnm", cos_out, turn_re) - dot("kn,ckm->cnm", sin_out, turn_im)
    series = series.reshape(narrow, seq_len) * (1.0 / size)
    back = lax.all_to_all(series, "seq", split_axis=1, concat_axis=0, tiled=True)
    return back.T


def on_device(loaded, counts, short_taps, filters, skip_gain, out_weight):
    my_index = lax.axis_index("seq")
    block_rows = filters.shape[0]
    parity = my_index % 2
    mate_count = from_partner(counts, "seq", 0)
    first_count = jnp.where(parity == 0, counts[0], mate_count[0])
    send_start = block_rows * (1 - parity)
    half = lax.dynamic_slice_in_dim(loaded, send_start, block_rows, 1)
    recv = from_partner(half, "seq", 0)
    first = jnp.where(parity == 0, loaded[:, :block_rows], recv)
    zeros = jnp.zeros_like(recv)
    second_src = jnp.where(
        parity == 0,
        jnp.concatenate([zeros, zeros, recv], axis=1),
        jnp.concatenate([zeros, loaded], axis=1),
    )
    second = lax.dynamic_slice_in_dim(second_src, 2 * block_rows - first_count, block_rows, 1)
    rows = jnp.arange(block_rows, dtype=jnp.int32)
    use_first = rows < first_count - block_rows * parity
    packed = jnp.where(use_first[None, :, None], first, second)
    rim_rows = shifted(packed[:, block_rows - 2 :], "seq", 1)
    extended = jnp.concatenate([rim_rows, packed], axis=1).astype(jnp.float32)
    filtered = sum(
        (
            short_taps[tap_index][:, None, :]
            * extended[:, 2 - tap_index : 2 - tap_index + block_rows]
            for tap_index in range(3)
        )
    )
    signal = filtered[0] * filtered[1]
    conv = channel_conv(signal, filters)
    gated = (filtered[2] * (conv + skip_gain[None, :] * signal)).astype(jnp.bfloat16)
    mixed = lax.psum_scatter(
        lax.dot_general(
            out_weight, gated, (((0,), (1,)), ((), ())), preferred_element_type=jnp.float32
        ),
        "chan",
        scatter_dimension=0,
        tiled=True,
    )
    return mixed.astype(jnp.bfloat16)


def solution(mesh):
    placed = (
        P(None, "seq", "chan"),
        P("seq"),
        P(None, None, "chan"),
        P("seq", "chan"),
        P("chan"),
        P("chan", None),
    )
    return jax.shard_map(
        on_device, mesh=mesh, in_specs=placed, out_specs=P("chan", "seq"), check_vma=False
    )
```

```python
import functools
import math

import jax
import jax.numpy as jnp
from jax import lax
from jax.sharding import PartitionSpec as P


def from_partner(value, axis, distance):
    mask = 2**distance
    pairs = [(source, source ^ mask) for source in range(lax.axis_size(axis))]
    return lax.ppermute(value, axis, pairs)


def shifted(block, axis, distance):
    devices = range(lax.axis_size(axis))
    route = [(i - distance, i) for i in devices if i - distance in devices]
    return lax.ppermute(block, axis, route)


def phase_table(out_ids, in_ids, modulus):
    product = out_ids[:, None] * in_ids[None, :] % modulus
    angle = product.astype(jnp.float32) * (2.0 * math.pi / modulus)
    return (jnp.cos(angle), jnp.sin(angle))


def channel_conv(signal, filters):
    stacked = jnp.swapaxes(jnp.stack([signal, filters]).astype(jnp.bfloat16), 1, 2)
    whole = lax.all_to_all(stacked, "seq", split_axis=1, concat_axis=2, tiled=True)
    streams, narrow, seq_len = whole.shape
    size = 2 * seq_len
    outer = 256
    inner = size // outer
    rows = seq_len // inner
    grid = whole.astype(jnp.float32).reshape(streams, narrow, rows, inner)
    outer_ids = jnp.arange(outer, dtype=jnp.int32)
    inner_ids = jnp.arange(inner, dtype=jnp.int32)
    cos_out, sin_out = phase_table(outer_ids, outer_ids[:rows], outer)
    cos_tw, sin_tw = phase_table(outer_ids, inner_ids, size)
    cos_in, sin_in = phase_table(inner_ids, inner_ids, inner)
    dot = functools.partial(jnp.einsum, precision=lax.Precision.HIGH)
    part_re = dot("kn,scnm->sckm", cos_out, grid)
    part_im = -dot("kn,scnm->sckm", sin_out, grid)
    twist_re = part_re * cos_tw + part_im * sin_tw
    twist_im = part_im * cos_tw - part_re * sin_tw
    spec_re = dot("sckm,mq->sckq", twist_re, cos_in) + dot("sckm,mq->sckq", twist_im, sin_in)
    spec_im = dot("sckm,mq->sckq", twist_im, cos_in) - dot("sckm,mq->sckq", twist_re, sin_in)
    prod_re = spec_re[0] * spec_re[1] - spec_im[0] * spec_im[1]
    prod_im = spec_re[0] * spec_im[1] + spec_im[0] * spec_re[1]
    back_re = dot("ckq,qm->ckm", prod_re, cos_in) - dot("ckq,qm->ckm", prod_im, sin_in)
    back_im = dot("ckq,qm->ckm", prod_im, cos_in) + dot("ckq,qm->ckm", prod_re, sin_in)
    turn_re = back_re * cos_tw - back_im * sin_tw
    turn_im = back_im * cos_tw + back_re * sin_tw
    series = dot("kn,ckm->cnm", cos_out, turn_re) - dot("kn,ckm->cnm", sin_out, turn_im)
    series = series.reshape(narrow, seq_len) * (1.0 / size)
    back = lax.all_to_all(series, "seq", split_axis=1, concat_axis=0, tiled=True)
    return back.T


def weight_columns(out_weight):
    count = lax.axis_size("chan")
    me = lax.axis_index("chan")
    rows, width = out_weight.shape[0], out_weight.shape[1] // count
    blocks = [lax.dynamic_slice_in_dim(out_weight, me * width, width, 1)]
    for step in range(1, count):
        piece = lax.dynamic_slice_in_dim(out_weight, (me + step) % count * width, width, 1)
        pairs = [(source, (source + step) % count) for source in range(count)]
        blocks.append(lax.ppermute(piece, "chan", pairs))
    order = (me - jnp.arange(count, dtype=jnp.int32)) % count
    return jnp.take(jnp.stack(blocks), order, axis=0).reshape(count * rows, width)


def on_device(loaded, counts, short_taps, filters, skip_gain, out_weight):
    my_index = lax.axis_index("seq")
    block_rows = filters.shape[0]
    parity = my_index % 2
    mate_count = from_partner(counts, "seq", 0)
    first_count = jnp.where(parity == 0, counts[0], mate_count[0])
    send_start = block_rows * (1 - parity)
    half = lax.dynamic_slice_in_dim(loaded, send_start, block_rows, 1)
    recv = from_partner(half, "seq", 0)
    first = jnp.where(parity == 0, loaded[:, :block_rows], recv)
    zeros = jnp.zeros_like(recv)
    second_src = jnp.where(
        parity == 0,
        jnp.concatenate([zeros, zeros, recv], axis=1),
        jnp.concatenate([zeros, loaded], axis=1),
    )
    second = lax.dynamic_slice_in_dim(second_src, 2 * block_rows - first_count, block_rows, 1)
    rows = jnp.arange(block_rows, dtype=jnp.int32)
    use_first = rows < first_count - block_rows * parity
    packed = jnp.where(use_first[None, :, None], first, second)
    rim_rows = shifted(packed[:, block_rows - 2 :], "seq", 1)
    extended = jnp.concatenate([rim_rows, packed], axis=1).astype(jnp.float32)
    filtered = sum(
        (
            short_taps[tap_index][:, None, :]
            * extended[:, 2 - tap_index : 2 - tap_index + block_rows]
            for tap_index in range(3)
        )
    )
    signal = filtered[0] * filtered[1]
    columns = weight_columns(out_weight)
    signal, columns = lax.optimization_barrier((signal, columns))
    conv = channel_conv(signal, filters)
    gated = (filtered[2] * (conv + skip_gain[None, :] * signal)).astype(jnp.bfloat16)
    every = lax.all_gather(gated, "chan", axis=1, tiled=True)
    mixed = lax.dot_general(
        columns, every, (((0,), (1,)), ((), ())), preferred_element_type=jnp.float32
    )
    return mixed.astype(jnp.bfloat16)


def solution(mesh):
    placed = (
        P(None, "seq", "chan"),
        P("seq"),
        P(None, None, "chan"),
        P("seq", "chan"),
        P("chan"),
        P("chan", None),
    )
    return jax.shard_map(
        on_device, mesh=mesh, in_specs=placed, out_specs=P("chan", "seq"), check_vma=False
    )
```

```python
import functools
import math

import jax
import jax.numpy as jnp
from jax import lax
from jax.sharding import PartitionSpec as P


def from_partner(value, axis, distance):
    mask = 2**distance
    pairs = [(source, source ^ mask) for source in range(lax.axis_size(axis))]
    return lax.ppermute(value, axis, pairs)


def shifted(block, axis, distance):
    devices = range(lax.axis_size(axis))
    route = [(i - distance, i) for i in devices if i - distance in devices]
    return lax.ppermute(block, axis, route)


def phase_table(out_ids, in_ids, modulus):
    product = out_ids[:, None] * in_ids[None, :] % modulus
    angle = product.astype(jnp.float32) * (2.0 * math.pi / modulus)
    return (jnp.cos(angle), jnp.sin(angle))


def channel_conv(signal, filters):
    stacked = jnp.swapaxes(jnp.stack([signal, filters]).astype(jnp.bfloat16), 1, 2)
    whole = lax.all_to_all(stacked, "seq", split_axis=1, concat_axis=2, tiled=True)
    streams, narrow, seq_len = whole.shape
    size = 2 * seq_len
    outer = 256
    inner = size // outer
    rows = seq_len // inner
    grid = whole.astype(jnp.float32).reshape(streams, narrow, rows, inner)
    outer_ids = jnp.arange(outer, dtype=jnp.int32)
    inner_ids = jnp.arange(inner, dtype=jnp.int32)
    cos_out, sin_out = phase_table(outer_ids, outer_ids[:rows], outer)
    cos_tw, sin_tw = phase_table(outer_ids, inner_ids, size)
    cos_in, sin_in = phase_table(inner_ids, inner_ids, inner)
    dot = functools.partial(jnp.einsum, precision=lax.Precision.HIGH)
    part_re = dot("kn,scnm->sckm", cos_out, grid)
    part_im = -dot("kn,scnm->sckm", sin_out, grid)
    twist_re = part_re * cos_tw + part_im * sin_tw
    twist_im = part_im * cos_tw - part_re * sin_tw
    spec_re = dot("sckm,mq->sckq", twist_re, cos_in) + dot("sckm,mq->sckq", twist_im, sin_in)
    spec_im = dot("sckm,mq->sckq", twist_im, cos_in) - dot("sckm,mq->sckq", twist_re, sin_in)
    prod_re = spec_re[0] * spec_re[1] - spec_im[0] * spec_im[1]
    prod_im = spec_re[0] * spec_im[1] + spec_im[0] * spec_re[1]
    back_re = dot("ckq,qm->ckm", prod_re, cos_in) - dot("ckq,qm->ckm", prod_im, sin_in)
    back_im = dot("ckq,qm->ckm", prod_im, cos_in) + dot("ckq,qm->ckm", prod_re, sin_in)
    turn_re = back_re * cos_tw - back_im * sin_tw
    turn_im = back_im * cos_tw + back_re * sin_tw
    series = dot("kn,ckm->cnm", cos_out, turn_re) - dot("kn,ckm->cnm", sin_out, turn_im)
    series = (series.reshape(narrow, seq_len) * (1.0 / size)).astype(jnp.bfloat16)
    back = lax.all_to_all(series, "seq", split_axis=1, concat_axis=0, tiled=True)
    return back.T.astype(jnp.float32)


def on_device(loaded, counts, short_taps, filters, skip_gain, out_weight):
    my_index = lax.axis_index("seq")
    block_rows = filters.shape[0]
    parity = my_index % 2
    mate_count = from_partner(counts, "seq", 0)
    first_count = jnp.where(parity == 0, counts[0], mate_count[0])
    send_start = block_rows * (1 - parity)
    half = lax.dynamic_slice_in_dim(loaded, send_start, block_rows, 1)
    recv = from_partner(half, "seq", 0)
    first = jnp.where(parity == 0, loaded[:, :block_rows], recv)
    zeros = jnp.zeros_like(recv)
    second_src = jnp.where(
        parity == 0,
        jnp.concatenate([zeros, zeros, recv], axis=1),
        jnp.concatenate([zeros, loaded], axis=1),
    )
    second = lax.dynamic_slice_in_dim(second_src, 2 * block_rows - first_count, block_rows, 1)
    rows = jnp.arange(block_rows, dtype=jnp.int32)
    use_first = rows < first_count - block_rows * parity
    packed = jnp.where(use_first[None, :, None], first, second)
    rim_rows = shifted(packed[:, block_rows - 2 :], "seq", 1)
    extended = jnp.concatenate([rim_rows, packed], axis=1).astype(jnp.float32)
    filtered = sum(
        (
            short_taps[tap_index][:, None, :]
            * extended[:, 2 - tap_index : 2 - tap_index + block_rows]
            for tap_index in range(3)
        )
    )
    signal = filtered[0] * filtered[1]
    conv = channel_conv(signal, filters)
    gated = (filtered[2] * (conv + skip_gain[None, :] * signal)).astype(jnp.bfloat16)
    mixed = lax.psum_scatter(
        lax.dot_general(
            out_weight, gated, (((0,), (1,)), ((), ())), preferred_element_type=jnp.float32
        ),
        "chan",
        scatter_dimension=0,
        tiled=True,
    )
    return mixed.astype(jnp.bfloat16)


def solution(mesh):
    placed = (
        P(None, "seq", "chan"),
        P("seq"),
        P(None, None, "chan"),
        P("seq", "chan"),
        P("chan"),
        P("chan", None),
    )
    return jax.shard_map(
        on_device, mesh=mesh, in_specs=placed, out_specs=P("chan", "seq"), check_vma=False
    )
```

```python
import functools
import math

import jax
import jax.numpy as jnp
from jax import lax
from jax.sharding import PartitionSpec as P


def from_partner(value, axis, distance):
    mask = 2**distance
    pairs = [(source, source ^ mask) for source in range(lax.axis_size(axis))]
    return lax.ppermute(value, axis, pairs)


def shifted(block, axis, distance):
    devices = range(lax.axis_size(axis))
    route = [(i - distance, i) for i in devices if i - distance in devices]
    return lax.ppermute(block, axis, route)


def phase_table(out_ids, in_ids, modulus):
    product = out_ids[:, None] * in_ids[None, :] % modulus
    angle = product.astype(jnp.float32) * (2.0 * math.pi / modulus)
    return (jnp.cos(angle), jnp.sin(angle))


def to_channels(values):
    narrow = jnp.swapaxes(values.astype(jnp.bfloat16), 0, 1)
    return lax.all_to_all(narrow, "seq", split_axis=0, concat_axis=1, tiled=True)


def spectrum(whole):
    narrow, seq_len = whole.shape
    size = 2 * seq_len
    outer = 256
    inner = size // outer
    rows = seq_len // inner
    grid = whole.astype(jnp.float32).reshape(narrow, rows, inner)
    outer_ids = jnp.arange(outer, dtype=jnp.int32)
    inner_ids = jnp.arange(inner, dtype=jnp.int32)
    cos_out, sin_out = phase_table(outer_ids, outer_ids[:rows], outer)
    cos_tw, sin_tw = phase_table(outer_ids, inner_ids, size)
    cos_in, sin_in = phase_table(inner_ids, inner_ids, inner)
    dot = functools.partial(jnp.einsum, precision=lax.Precision.HIGH)
    part_re = dot("kn,cnm->ckm", cos_out, grid)
    part_im = -dot("kn,cnm->ckm", sin_out, grid)
    twist_re = part_re * cos_tw + part_im * sin_tw
    twist_im = part_im * cos_tw - part_re * sin_tw
    spec_re = dot("ckm,mq->ckq", twist_re, cos_in) + dot("ckm,mq->ckq", twist_im, sin_in)
    spec_im = dot("ckm,mq->ckq", twist_im, cos_in) - dot("ckm,mq->ckq", twist_re, sin_in)
    return spec_re, spec_im


def channel_conv(signal, filter_spec):
    whole = to_channels(signal)
    narrow, seq_len = whole.shape
    size = 2 * seq_len
    outer = 256
    inner = size // outer
    rows = seq_len // inner
    outer_ids = jnp.arange(outer, dtype=jnp.int32)
    inner_ids = jnp.arange(inner, dtype=jnp.int32)
    cos_out, sin_out = phase_table(outer_ids, outer_ids[:rows], outer)
    cos_tw, sin_tw = phase_table(outer_ids, inner_ids, size)
    cos_in, sin_in = phase_table(inner_ids, inner_ids, inner)
    dot = functools.partial(jnp.einsum, precision=lax.Precision.HIGH)
    sig_re, sig_im = spectrum(whole)
    filt_re, filt_im = filter_spec
    prod_re = sig_re * filt_re - sig_im * filt_im
    prod_im = sig_re * filt_im + sig_im * filt_re
    back_re = dot("ckq,qm->ckm", prod_re, cos_in) - dot("ckq,qm->ckm", prod_im, sin_in)
    back_im = dot("ckq,qm->ckm", prod_im, cos_in) + dot("ckq,qm->ckm", prod_re, sin_in)
    turn_re = back_re * cos_tw - back_im * sin_tw
    turn_im = back_im * cos_tw + back_re * sin_tw
    series = dot("kn,ckm->cnm", cos_out, turn_re) - dot("kn,ckm->cnm", sin_out, turn_im)
    series = (series.reshape(narrow, seq_len) * (1.0 / size)).astype(jnp.bfloat16)
    back = lax.all_to_all(series, "seq", split_axis=1, concat_axis=0, tiled=True)
    return back.T.astype(jnp.float32)


def on_device(loaded, counts, short_taps, filters, skip_gain, out_weight):
    my_index = lax.axis_index("seq")
    block_rows = filters.shape[0]
    filter_spec = spectrum(to_channels(filters))
    parity = my_index % 2
    mate_count = from_partner(counts, "seq", 0)
    first_count = jnp.where(parity == 0, counts[0], mate_count[0])
    send_start = block_rows * (1 - parity)
    half = lax.dynamic_slice_in_dim(loaded, send_start, block_rows, 1)
    recv = from_partner(half, "seq", 0)
    first = jnp.where(parity == 0, loaded[:, :block_rows], recv)
    zeros = jnp.zeros_like(recv)
    second_src = jnp.where(
        parity == 0,
        jnp.concatenate([zeros, zeros, recv], axis=1),
        jnp.concatenate([zeros, loaded], axis=1),
    )
    second = lax.dynamic_slice_in_dim(second_src, 2 * block_rows - first_count, block_rows, 1)
    rows = jnp.arange(block_rows, dtype=jnp.int32)
    use_first = rows < first_count - block_rows * parity
    packed = jnp.where(use_first[None, :, None], first, second)
    rim_rows = shifted(packed[:, block_rows - 2 :], "seq", 1)
    extended = jnp.concatenate([rim_rows, packed], axis=1).astype(jnp.float32)
    filtered = sum(
        (
            short_taps[tap_index][:, None, :]
            * extended[:, 2 - tap_index : 2 - tap_index + block_rows]
            for tap_index in range(3)
        )
    )
    signal = filtered[0] * filtered[1]
    conv = channel_conv(signal, filter_spec)
    gated = (filtered[2] * (conv + skip_gain[None, :] * signal)).astype(jnp.bfloat16)
    mixed = lax.psum_scatter(
        lax.dot_general(
            out_weight, gated, (((0,), (1,)), ((), ())), preferred_element_type=jnp.float32
        ),
        "chan",
        scatter_dimension=0,
        tiled=True,
    )
    return mixed.astype(jnp.bfloat16)


def solution(mesh):
    placed = (
        P(None, "seq", "chan"),
        P("seq"),
        P(None, None, "chan"),
        P("seq", "chan"),
        P("chan"),
        P("chan", None),
    )
    return jax.shard_map(
        on_device, mesh=mesh, in_specs=placed, out_specs=P("chan", "seq"), check_vma=False
    )
```

```python
import functools
import math

import jax
import jax.numpy as jnp
from jax import lax
from jax.sharding import PartitionSpec as P


def from_partner(value, axis, distance):
    mask = 2**distance
    pairs = [(source, source ^ mask) for source in range(lax.axis_size(axis))]
    return lax.ppermute(value, axis, pairs)


def shifted(block, axis, distance):
    devices = range(lax.axis_size(axis))
    route = [(i - distance, i) for i in devices if i - distance in devices]
    return lax.ppermute(block, axis, route)


def phase_table(out_ids, in_ids, modulus):
    product = out_ids[:, None] * in_ids[None, :] % modulus
    angle = product.astype(jnp.float32) * (2.0 * math.pi / modulus)
    return (jnp.cos(angle), jnp.sin(angle))


def channel_conv(signal, filters):
    stacked = jnp.swapaxes(jnp.stack([signal, filters]).astype(jnp.bfloat16), 1, 2)
    whole = lax.all_to_all(stacked, "seq", split_axis=1, concat_axis=2, tiled=True)
    streams, narrow, seq_len = whole.shape
    size = 2 * seq_len
    outer = 256
    inner = size // outer
    rows = seq_len // inner
    grid = whole.astype(jnp.float32).reshape(streams, narrow, rows, inner)
    outer_ids = jnp.arange(outer, dtype=jnp.int32)
    inner_ids = jnp.arange(inner, dtype=jnp.int32)
    cos_out, sin_out = phase_table(outer_ids, outer_ids[:rows], outer)
    cos_tw, sin_tw = phase_table(outer_ids, inner_ids, size)
    cos_in, sin_in = phase_table(inner_ids, inner_ids, inner)
    dot = functools.partial(jnp.einsum, precision=lax.Precision.HIGH)
    part_re = dot("kn,scnm->sckm", cos_out, grid)
    part_im = -dot("kn,scnm->sckm", sin_out, grid)
    twist_re = part_re * cos_tw + part_im * sin_tw
    twist_im = part_im * cos_tw - part_re * sin_tw
    spec_re = dot("sckm,mq->sckq", twist_re, cos_in) + dot("sckm,mq->sckq", twist_im, sin_in)
    spec_im = dot("sckm,mq->sckq", twist_im, cos_in) - dot("sckm,mq->sckq", twist_re, sin_in)
    prod_re = spec_re[0] * spec_re[1] - spec_im[0] * spec_im[1]
    prod_im = spec_re[0] * spec_im[1] + spec_im[0] * spec_re[1]
    back_re = dot("ckq,qm->ckm", prod_re, cos_in) - dot("ckq,qm->ckm", prod_im, sin_in)
    back_im = dot("ckq,qm->ckm", prod_im, cos_in) + dot("ckq,qm->ckm", prod_re, sin_in)
    turn_re = back_re * cos_tw - back_im * sin_tw
    turn_im = back_im * cos_tw + back_re * sin_tw
    series = dot("kn,ckm->cnm", cos_out, turn_re) - dot("kn,ckm->cnm", sin_out, turn_im)
    series = (series.reshape(narrow, seq_len) * (1.0 / size)).astype(jnp.bfloat16)
    back = lax.all_to_all(series, "seq", split_axis=1, concat_axis=0, tiled=True)
    return back.T.astype(jnp.float32)


def on_device(loaded, counts, short_taps, filters, skip_gain, out_weight):
    my_index = lax.axis_index("seq")
    block_rows = filters.shape[0]
    parity = my_index % 2
    mate_count = from_partner(counts, "seq", 0)
    first_count = jnp.where(parity == 0, counts[0], mate_count[0])
    send_start = block_rows * (1 - parity)
    half = lax.dynamic_slice_in_dim(loaded, send_start, block_rows, 1)
    recv = from_partner(half, "seq", 0)
    first = jnp.where(parity == 0, loaded[:, :block_rows], recv)
    zeros = jnp.zeros_like(recv)
    second_src = jnp.where(
        parity == 0,
        jnp.concatenate([zeros, zeros, recv], axis=1),
        jnp.concatenate([zeros, loaded], axis=1),
    )
    second = lax.dynamic_slice_in_dim(second_src, 2 * block_rows - first_count, block_rows, 1)
    rows = jnp.arange(block_rows, dtype=jnp.int32)
    use_first = rows < first_count - block_rows * parity
    packed = jnp.where(use_first[None, :, None], first, second)
    rim_rows = shifted(packed[:, block_rows - 2 :], "seq", 1)
    extended = jnp.concatenate([rim_rows, packed], axis=1).astype(jnp.float32)
    filtered = sum(
        (
            short_taps[tap_index][:, None, :]
            * extended[:, 2 - tap_index : 2 - tap_index + block_rows]
            for tap_index in range(3)
        )
    )
    signal = filtered[0] * filtered[1]
    conv = channel_conv(signal, filters)
    gated = (filtered[2] * (conv + skip_gain[None, :] * signal)).astype(jnp.bfloat16)
    cores = lax.axis_size("core")
    chips = lax.axis_size("chip")
    rows, width = out_weight.shape[0], out_weight.shape[1] // (cores * chips)
    by_core = jnp.swapaxes(out_weight.reshape(rows, chips, cores, width), 1, 2)
    partial = lax.dot_general(
        by_core.reshape(rows, -1), gated, (((0,), (1,)), ((), ())),
        preferred_element_type=jnp.float32,
    )
    half = lax.psum_scatter(partial, "core", scatter_dimension=0, tiled=True)
    mixed = lax.psum_scatter(half, "chip", scatter_dimension=0, tiled=True)
    return mixed.astype(jnp.bfloat16)


def solution(mesh):
    cores = 2
    devices = mesh.devices.reshape(mesh.shape["seq"], mesh.shape["chan"] // cores, cores)
    split = jax.sharding.Mesh(devices, ("seq", "chip", "core"))
    chan = ("chip", "core")
    placed = (
        P(None, "seq", chan),
        P("seq"),
        P(None, None, chan),
        P("seq", chan),
        P(chan),
        P(chan, None),
    )
    return jax.shard_map(
        on_device, mesh=split, in_specs=placed, out_specs=P(chan, "seq"), check_vma=False
    )
```

```python
import functools
import math

import jax
import jax.numpy as jnp
from jax import lax
from jax.sharding import PartitionSpec as P


def from_partner(value, axis, distance):
    mask = 2**distance
    pairs = [(source, source ^ mask) for source in range(lax.axis_size(axis))]
    return lax.ppermute(value, axis, pairs)


def shifted(block, axis, distance):
    devices = range(lax.axis_size(axis))
    route = [(i - distance, i) for i in devices if i - distance in devices]
    return lax.ppermute(block, axis, route)


def phase_table(out_ids, in_ids, modulus):
    product = out_ids[:, None] * in_ids[None, :] % modulus
    angle = product.astype(jnp.float32) * (2.0 * math.pi / modulus)
    return (jnp.cos(angle), jnp.sin(angle))


def channel_conv(signal, filters, blocks):
    stacked = jnp.swapaxes(jnp.stack([signal, filters]).astype(jnp.bfloat16), 1, 2)
    whole = lax.all_to_all(stacked, "seq", split_axis=1, concat_axis=2, tiled=True)
    streams, narrow, seq_len = whole.shape
    size = 2 * seq_len
    outer = 256
    inner = size // outer
    rows = seq_len // inner
    grid = whole.astype(jnp.float32).reshape(streams, narrow, rows, inner)
    outer_ids = jnp.arange(outer, dtype=jnp.int32)
    inner_ids = jnp.arange(inner, dtype=jnp.int32)
    cos_out, sin_out = phase_table(outer_ids, outer_ids[:rows], outer)
    cos_tw, sin_tw = phase_table(outer_ids, inner_ids, size)
    cos_in, sin_in = phase_table(inner_ids, inner_ids, inner)
    dot = functools.partial(jnp.einsum, precision=lax.Precision.HIGH)
    part_re = dot("kn,scnm->sckm", cos_out, grid)
    part_im = -dot("kn,scnm->sckm", sin_out, grid)
    twist_re = part_re * cos_tw + part_im * sin_tw
    twist_im = part_im * cos_tw - part_re * sin_tw
    spec_re = dot("sckm,mq->sckq", twist_re, cos_in) + dot("sckm,mq->sckq", twist_im, sin_in)
    spec_im = dot("sckm,mq->sckq", twist_im, cos_in) - dot("sckm,mq->sckq", twist_re, sin_in)
    prod_re = spec_re[0] * spec_re[1] - spec_im[0] * spec_im[1]
    prod_im = spec_re[0] * spec_im[1] + spec_im[0] * spec_re[1]
    back_re = dot("ckq,qm->ckm", prod_re, cos_in) - dot("ckq,qm->ckm", prod_im, sin_in)
    back_im = dot("ckq,qm->ckm", prod_im, cos_in) + dot("ckq,qm->ckm", prod_re, sin_in)
    turn_re = back_re * cos_tw - back_im * sin_tw
    turn_im = back_im * cos_tw + back_re * sin_tw
    series = dot("kn,ckm->cnm", cos_out, turn_re) - dot("kn,ckm->cnm", sin_out, turn_im)
    series = (series.reshape(narrow, seq_len) * (1.0 / size)).astype(jnp.bfloat16)
    series, blocks = lax.optimization_barrier((series, blocks))
    back = lax.all_to_all(series, "seq", split_axis=1, concat_axis=0, tiled=True)
    return back.T.astype(jnp.float32), blocks


def weight_blocks(out_weight):
    count = lax.axis_size("chan")
    me = lax.axis_index("chan")
    width = out_weight.shape[1] // count
    blocks = [lax.dynamic_slice_in_dim(out_weight, me * width, width, 1)]
    for step in range(1, count):
        piece = lax.dynamic_slice_in_dim(out_weight, (me + step) % count * width, width, 1)
        pairs = [(source, (source + step) % count) for source in range(count)]
        blocks.append(lax.ppermute(piece, "chan", pairs))
    return blocks


def project(blocks, every):
    count = len(blocks)
    me = lax.axis_index("chan")
    width = every.shape[1] // count
    total = None
    for step, block in enumerate(blocks):
        part = lax.dynamic_slice_in_dim(every, (me - step) % count * width, width, 1)
        term = lax.dot_general(
            block, part, (((0,), (1,)), ((), ())), preferred_element_type=jnp.float32
        )
        total = term if total is None else total + term
    return total


def on_device(loaded, counts, short_taps, filters, skip_gain, out_weight):
    my_index = lax.axis_index("seq")
    block_rows = filters.shape[0]
    parity = my_index % 2
    mate_count = from_partner(counts, "seq", 0)
    first_count = jnp.where(parity == 0, counts[0], mate_count[0])
    send_start = block_rows * (1 - parity)
    half = lax.dynamic_slice_in_dim(loaded, send_start, block_rows, 1)
    recv = from_partner(half, "seq", 0)
    first = jnp.where(parity == 0, loaded[:, :block_rows], recv)
    zeros = jnp.zeros_like(recv)
    second_src = jnp.where(
        parity == 0,
        jnp.concatenate([zeros, zeros, recv], axis=1),
        jnp.concatenate([zeros, loaded], axis=1),
    )
    second = lax.dynamic_slice_in_dim(second_src, 2 * block_rows - first_count, block_rows, 1)
    rows = jnp.arange(block_rows, dtype=jnp.int32)
    use_first = rows < first_count - block_rows * parity
    packed = jnp.where(use_first[None, :, None], first, second)
    rim_rows = shifted(packed[:, block_rows - 2 :], "seq", 1)
    extended = jnp.concatenate([rim_rows, packed], axis=1).astype(jnp.float32)
    filtered = sum(
        (
            short_taps[tap_index][:, None, :]
            * extended[:, 2 - tap_index : 2 - tap_index + block_rows]
            for tap_index in range(3)
        )
    )
    signal = filtered[0] * filtered[1]
    conv, blocks = channel_conv(signal, filters, weight_blocks(out_weight))
    gated = (filtered[2] * (conv + skip_gain[None, :] * signal)).astype(jnp.bfloat16)
    every = lax.all_gather(gated, "chan", axis=1, tiled=True)
    mixed = project(blocks, every)
    return mixed.astype(jnp.bfloat16)


def solution(mesh):
    placed = (
        P(None, "seq", "chan"),
        P("seq"),
        P(None, None, "chan"),
        P("seq", "chan"),
        P("chan"),
        P("chan", None),
    )
    return jax.shard_map(
        on_device, mesh=mesh, in_specs=placed, out_specs=P("chan", "seq"), check_vma=False
    )
```

```python
import functools
import math

import jax
import jax.numpy as jnp
from jax import lax
from jax.sharding import PartitionSpec as P


def from_partner(value, axis, distance):
    mask = 2**distance
    pairs = [(source, source ^ mask) for source in range(lax.axis_size(axis))]
    return lax.ppermute(value, axis, pairs)


def shifted(block, axis, distance):
    devices = range(lax.axis_size(axis))
    route = [(i - distance, i) for i in devices if i - distance in devices]
    return lax.ppermute(block, axis, route)


def phase_table(out_ids, in_ids, modulus):
    product = out_ids[:, None] * in_ids[None, :] % modulus
    angle = product.astype(jnp.float32) * (2.0 * math.pi / modulus)
    return (jnp.cos(angle), jnp.sin(angle))


def channel_conv(signal, filters, blocks):
    stacked = jnp.swapaxes(jnp.stack([signal, filters]).astype(jnp.bfloat16), 1, 2)
    whole = lax.all_to_all(stacked, "seq", split_axis=1, concat_axis=2, tiled=True)
    streams, narrow, seq_len = whole.shape
    size = 2 * seq_len
    outer = 256
    inner = size // outer
    rows = seq_len // inner
    grid = whole.astype(jnp.float32).reshape(streams, narrow, rows, inner)
    outer_ids = jnp.arange(outer, dtype=jnp.int32)
    inner_ids = jnp.arange(inner, dtype=jnp.int32)
    cos_out, sin_out = phase_table(outer_ids, outer_ids[:rows], outer)
    cos_tw, sin_tw = phase_table(outer_ids, inner_ids, size)
    cos_in, sin_in = phase_table(inner_ids, inner_ids, inner)
    dot = functools.partial(jnp.einsum, precision=lax.Precision.HIGH)
    part_re = dot("kn,scnm->sckm", cos_out, grid)
    part_im = -dot("kn,scnm->sckm", sin_out, grid)
    twist_re = part_re * cos_tw + part_im * sin_tw
    twist_im = part_im * cos_tw - part_re * sin_tw
    spec_re = dot("sckm,mq->sckq", twist_re, cos_in) + dot("sckm,mq->sckq", twist_im, sin_in)
    spec_im = dot("sckm,mq->sckq", twist_im, cos_in) - dot("sckm,mq->sckq", twist_re, sin_in)
    prod_re = spec_re[0] * spec_re[1] - spec_im[0] * spec_im[1]
    prod_im = spec_re[0] * spec_im[1] + spec_im[0] * spec_re[1]
    back_re = dot("ckq,qm->ckm", prod_re, cos_in) - dot("ckq,qm->ckm", prod_im, sin_in)
    back_im = dot("ckq,qm->ckm", prod_im, cos_in) + dot("ckq,qm->ckm", prod_re, sin_in)
    turn_re = back_re * cos_tw - back_im * sin_tw
    turn_im = back_im * cos_tw + back_re * sin_tw
    series = dot("kn,ckm->cnm", cos_out, turn_re) - dot("kn,ckm->cnm", sin_out, turn_im)
    series = (series.reshape(narrow, seq_len) * (1.0 / size)).astype(jnp.bfloat16)
    series, blocks = lax.optimization_barrier((series, blocks))
    back = lax.all_to_all(series, "seq", split_axis=1, concat_axis=0, tiled=True)
    return back.T.astype(jnp.float32), blocks


def weight_blocks(out_weight):
    count = lax.axis_size("chan")
    me = lax.axis_index("chan")
    width = out_weight.shape[1] // count
    blocks = [lax.dynamic_slice_in_dim(out_weight, me * width, width, 1)]
    for step in range(1, count):
        piece = lax.dynamic_slice_in_dim(out_weight, (me + step) % count * width, width, 1)
        pairs = [(source, (source + step) % count) for source in range(count)]
        blocks.append(lax.ppermute(piece, "chan", pairs))
    return blocks


def project(blocks, every):
    count = len(blocks)
    me = lax.axis_index("chan")
    order = (me - jnp.arange(count, dtype=jnp.int32)) % count
    columns = jnp.take(jnp.stack(blocks), order, axis=0)
    columns = columns.reshape(count * blocks[0].shape[0], blocks[0].shape[1])
    return lax.dot_general(
        columns, every, (((0,), (1,)), ((), ())), preferred_element_type=jnp.float32
    )


def on_device(loaded, counts, short_taps, filters, skip_gain, out_weight):
    my_index = lax.axis_index("seq")
    block_rows = filters.shape[0]
    parity = my_index % 2
    mate_count = from_partner(counts, "seq", 0)
    first_count = jnp.where(parity == 0, counts[0], mate_count[0])
    send_start = block_rows * (1 - parity)
    half = lax.dynamic_slice_in_dim(loaded, send_start, block_rows, 1)
    recv = from_partner(half, "seq", 0)
    first = jnp.where(parity == 0, loaded[:, :block_rows], recv)
    zeros = jnp.zeros_like(recv)
    second_src = jnp.where(
        parity == 0,
        jnp.concatenate([zeros, zeros, recv], axis=1),
        jnp.concatenate([zeros, loaded], axis=1),
    )
    second = lax.dynamic_slice_in_dim(second_src, 2 * block_rows - first_count, block_rows, 1)
    rows = jnp.arange(block_rows, dtype=jnp.int32)
    use_first = rows < first_count - block_rows * parity
    packed = jnp.where(use_first[None, :, None], first, second)
    rim_rows = shifted(packed[:, block_rows - 2 :], "seq", 1)
    extended = jnp.concatenate([rim_rows, packed], axis=1).astype(jnp.float32)
    filtered = sum(
        (
            short_taps[tap_index][:, None, :]
            * extended[:, 2 - tap_index : 2 - tap_index + block_rows]
            for tap_index in range(3)
        )
    )
    signal = filtered[0] * filtered[1]
    conv, blocks = channel_conv(signal, filters, weight_blocks(out_weight))
    gated = (filtered[2] * (conv + skip_gain[None, :] * signal)).astype(jnp.bfloat16)
    every = lax.all_gather(gated, "chan", axis=1, tiled=True)
    mixed = project(blocks, every)
    return mixed.astype(jnp.bfloat16)


def solution(mesh):
    placed = (
        P(None, "seq", "chan"),
        P("seq"),
        P(None, None, "chan"),
        P("seq", "chan"),
        P("chan"),
        P("chan", None),
    )
    return jax.shard_map(
        on_device, mesh=mesh, in_specs=placed, out_specs=P("chan", "seq"), check_vma=False
    )
```

```python
import functools
import math

import jax
import jax.numpy as jnp
from jax import lax
from jax.sharding import PartitionSpec as P


def from_partner(value, axis, distance):
    mask = 2**distance
    pairs = [(source, source ^ mask) for source in range(lax.axis_size(axis))]
    return lax.ppermute(value, axis, pairs)


def shifted(block, axis, distance):
    devices = range(lax.axis_size(axis))
    route = [(i - distance, i) for i in devices if i - distance in devices]
    return lax.ppermute(block, axis, route)


def phase_table(out_ids, in_ids, modulus):
    product = out_ids[:, None] * in_ids[None, :] % modulus
    angle = product.astype(jnp.float32) * (2.0 * math.pi / modulus)
    return (jnp.cos(angle), jnp.sin(angle))


def channel_conv(signal, filters, blocks):
    stacked = jnp.swapaxes(jnp.stack([signal, filters]).astype(jnp.bfloat16), 1, 2)
    whole = lax.all_to_all(stacked, "seq", split_axis=1, concat_axis=2, tiled=True)
    streams, narrow, seq_len = whole.shape
    size = 2 * seq_len
    outer = 256
    inner = size // outer
    rows = seq_len // inner
    grid = whole.astype(jnp.float32).reshape(streams, narrow, rows, inner)
    outer_ids = jnp.arange(outer, dtype=jnp.int32)
    inner_ids = jnp.arange(inner, dtype=jnp.int32)
    cos_out, sin_out = phase_table(outer_ids, outer_ids[:rows], outer)
    cos_tw, sin_tw = phase_table(outer_ids, inner_ids, size)
    cos_in, sin_in = phase_table(inner_ids, inner_ids, inner)
    dot = functools.partial(jnp.einsum, precision=lax.Precision.HIGH)
    part_re = dot("kn,scnm->sckm", cos_out, grid)
    part_im = -dot("kn,scnm->sckm", sin_out, grid)
    twist_re = part_re * cos_tw + part_im * sin_tw
    twist_im = part_im * cos_tw - part_re * sin_tw
    spec_re = dot("sckm,mq->sckq", twist_re, cos_in) + dot("sckm,mq->sckq", twist_im, sin_in)
    spec_im = dot("sckm,mq->sckq", twist_im, cos_in) - dot("sckm,mq->sckq", twist_re, sin_in)
    prod_re = spec_re[0] * spec_re[1] - spec_im[0] * spec_im[1]
    prod_im = spec_re[0] * spec_im[1] + spec_im[0] * spec_re[1]
    back_re = dot("ckq,qm->ckm", prod_re, cos_in) - dot("ckq,qm->ckm", prod_im, sin_in)
    back_im = dot("ckq,qm->ckm", prod_im, cos_in) + dot("ckq,qm->ckm", prod_re, sin_in)
    turn_re = back_re * cos_tw - back_im * sin_tw
    turn_im = back_im * cos_tw + back_re * sin_tw
    series = dot("kn,ckm->cnm", cos_out, turn_re) - dot("kn,ckm->cnm", sin_out, turn_im)
    series = (series.reshape(narrow, seq_len) * (1.0 / size)).astype(jnp.bfloat16)
    series, blocks = lax.optimization_barrier((series, blocks))
    halves = jnp.split(series, 2, axis=0)
    return halves, blocks


def to_positions(half):
    back = lax.all_to_all(half, "seq", split_axis=1, concat_axis=0, tiled=True)
    return back.T.astype(jnp.float32)


def weight_blocks(out_weight):
    count = lax.axis_size("chan")
    me = lax.axis_index("chan")
    width = out_weight.shape[1] // count
    blocks = [lax.dynamic_slice_in_dim(out_weight, me * width, width, 1)]
    for step in range(1, count):
        piece = lax.dynamic_slice_in_dim(out_weight, (me + step) % count * width, width, 1)
        pairs = [(source, (source + step) % count) for source in range(count)]
        blocks.append(lax.ppermute(piece, "chan", pairs))
    return blocks


def project(blocks, everys, seq_count):
    count = len(blocks)
    me = lax.axis_index("chan")
    order = (me - jnp.arange(count, dtype=jnp.int32)) % count
    columns = jnp.take(jnp.stack(blocks), order, axis=0)
    rows, width = blocks[0].shape
    columns = columns.reshape(count, seq_count, 2, rows // seq_count // 2, width)
    total = None
    for half, every in enumerate(everys):
        part = columns[:, :, half].reshape(-1, width)
        term = lax.dot_general(
            part, every, (((0,), (1,)), ((), ())), preferred_element_type=jnp.float32
        )
        total = term if total is None else total + term
    return total


def on_device(loaded, counts, short_taps, filters, skip_gain, out_weight):
    my_index = lax.axis_index("seq")
    block_rows = filters.shape[0]
    parity = my_index % 2
    mate_count = from_partner(counts, "seq", 0)
    first_count = jnp.where(parity == 0, counts[0], mate_count[0])
    send_start = block_rows * (1 - parity)
    half = lax.dynamic_slice_in_dim(loaded, send_start, block_rows, 1)
    recv = from_partner(half, "seq", 0)
    first = jnp.where(parity == 0, loaded[:, :block_rows], recv)
    zeros = jnp.zeros_like(recv)
    second_src = jnp.where(
        parity == 0,
        jnp.concatenate([zeros, zeros, recv], axis=1),
        jnp.concatenate([zeros, loaded], axis=1),
    )
    second = lax.dynamic_slice_in_dim(second_src, 2 * block_rows - first_count, block_rows, 1)
    rows = jnp.arange(block_rows, dtype=jnp.int32)
    use_first = rows < first_count - block_rows * parity
    packed = jnp.where(use_first[None, :, None], first, second)
    rim_rows = shifted(packed[:, block_rows - 2 :], "seq", 1)
    extended = jnp.concatenate([rim_rows, packed], axis=1).astype(jnp.float32)
    filtered = sum(
        (
            short_taps[tap_index][:, None, :]
            * extended[:, 2 - tap_index : 2 - tap_index + block_rows]
            for tap_index in range(3)
        )
    )
    signal = filtered[0] * filtered[1]
    conv, blocks = channel_conv(signal, filters, weight_blocks(out_weight))
    seq_count = lax.axis_size("seq")
    narrow = filtered.shape[-1] // seq_count // 2

    def halve(values, half):
        shape = values.shape[:-1]
        return values.reshape(*shape, seq_count, 2, narrow)[..., half, :].reshape(*shape, -1)

    everys = []
    later = conv[1]
    for half in range(2):
        if half == 0:
            conv_half = to_positions(conv[0])
        else:
            conv_half = to_positions(later)
        gated = (
            halve(filtered[2], half)
            * (conv_half + halve(skip_gain, half)[None, :] * halve(signal, half))
        ).astype(jnp.bfloat16)
        if half == 0:
            gated, later = lax.optimization_barrier((gated, later))
        everys.append(lax.all_gather(gated, "chan", axis=1, tiled=True))
    mixed = project(blocks, everys, seq_count)
    return mixed.astype(jnp.bfloat16)


def solution(mesh):
    placed = (
        P(None, "seq", "chan"),
        P("seq"),
        P(None, None, "chan"),
        P("seq", "chan"),
        P("chan"),
        P("chan", None),
    )
    return jax.shard_map(
        on_device, mesh=mesh, in_specs=placed, out_specs=P("chan", "seq"), check_vma=False
    )
```

```python
import functools
import math

import jax
import jax.numpy as jnp
from jax import lax
from jax.sharding import PartitionSpec as P


def from_partner(value, axis, distance):
    mask = 2**distance
    pairs = [(source, source ^ mask) for source in range(lax.axis_size(axis))]
    return lax.ppermute(value, axis, pairs)


def shifted(block, axis, distance):
    devices = range(lax.axis_size(axis))
    route = [(i - distance, i) for i in devices if i - distance in devices]
    return lax.ppermute(block, axis, route)


def phase_table(out_ids, in_ids, modulus):
    product = out_ids[:, None] * in_ids[None, :] % modulus
    angle = product.astype(jnp.float32) * (2.0 * math.pi / modulus)
    return (jnp.cos(angle), jnp.sin(angle))


def channel_conv(signal, filters, blocks):
    stacked = jnp.swapaxes(jnp.stack([signal, filters]).astype(jnp.bfloat16), 1, 2)
    whole = lax.all_to_all(stacked, "seq", split_axis=1, concat_axis=2, tiled=True)
    streams, narrow, seq_len = whole.shape
    size = 2 * seq_len
    outer = 256
    inner = size // outer
    rows = seq_len // inner
    grid = whole.astype(jnp.float32).reshape(streams, narrow, rows, inner)
    outer_ids = jnp.arange(outer, dtype=jnp.int32)
    inner_ids = jnp.arange(inner, dtype=jnp.int32)
    cos_out, sin_out = phase_table(outer_ids, outer_ids[:rows], outer)
    cos_tw, sin_tw = phase_table(outer_ids, inner_ids, size)
    cos_in, sin_in = phase_table(inner_ids, inner_ids, inner)
    dot = functools.partial(jnp.einsum, precision=lax.Precision.HIGH)
    part_re = dot("kn,scnm->sckm", cos_out, grid)
    part_im = -dot("kn,scnm->sckm", sin_out, grid)
    twist_re = part_re * cos_tw + part_im * sin_tw
    twist_im = part_im * cos_tw - part_re * sin_tw
    spec_re = dot("sckm,mq->sckq", twist_re, cos_in) + dot("sckm,mq->sckq", twist_im, sin_in)
    spec_im = dot("sckm,mq->sckq", twist_im, cos_in) - dot("sckm,mq->sckq", twist_re, sin_in)
    prod_re = spec_re[0] * spec_re[1] - spec_im[0] * spec_im[1]
    prod_im = spec_re[0] * spec_im[1] + spec_im[0] * spec_re[1]
    back_re = dot("ckq,qm->ckm", prod_re, cos_in) - dot("ckq,qm->ckm", prod_im, sin_in)
    back_im = dot("ckq,qm->ckm", prod_im, cos_in) + dot("ckq,qm->ckm", prod_re, sin_in)
    turn_re = back_re * cos_tw - back_im * sin_tw
    turn_im = back_im * cos_tw + back_re * sin_tw
    series = dot("kn,ckm->cnm", cos_out, turn_re) - dot("kn,ckm->cnm", sin_out, turn_im)
    series = (series.reshape(narrow, seq_len) * (1.0 / size)).astype(jnp.bfloat16)
    series, blocks = lax.optimization_barrier((series, blocks))
    back = lax.all_to_all(series, "seq", split_axis=1, concat_axis=0, tiled=True)
    return back.T.astype(jnp.float32), blocks


def weight_blocks(out_weight):
    count = lax.axis_size("chan")
    me = lax.axis_index("chan")
    width = out_weight.shape[1] // count
    blocks = [lax.dynamic_slice_in_dim(out_weight, me * width, width, 1)]
    for step in range(1, count):
        piece = lax.dynamic_slice_in_dim(out_weight, (me + step) % count * width, width, 1)
        pairs = [(source, (source + step) % count) for source in range(count)]
        blocks.append(lax.ppermute(piece, "chan", pairs))
    return blocks


def project(blocks, every):
    count = len(blocks)
    me = lax.axis_index("chan")
    order = (me - jnp.arange(count, dtype=jnp.int32)) % count
    columns = jnp.take(jnp.stack(blocks), order, axis=0)
    columns = columns.reshape(count * blocks[0].shape[0], blocks[0].shape[1])
    return lax.dot_general(
        columns, every, (((0,), (1,)), ((), ())), preferred_element_type=jnp.float32
    )


def rim_of(loaded, count, mate_count, first_count, parity, block_rows):
    pair_rows = 2 * block_rows
    front = jnp.concatenate([jnp.zeros_like(loaded[:, :2]), loaded], axis=1)
    tail_start = jnp.where(parity == 0, block_rows - 2, pair_rows - 2 - mate_count)
    sent_near = lax.dynamic_slice_in_dim(front, tail_start + 2, 2, 1)
    near = shifted(sent_near, "seq", 1)
    far = shifted(loaded[:, pair_rows - 2 :], "seq", 2)
    far_count = shifted(count[None], "seq", 2)[0]
    own_rows = lax.dynamic_slice_in_dim(front, block_rows - first_count, 2, 1)
    split = jnp.where(parity == 0, far_count, first_count)
    base = jnp.where(parity == 0, pair_rows - 2, block_rows - 2)
    first_part = jnp.where(parity == 0, far, near)
    second_part = jnp.where(parity == 0, near, own_rows)
    positions = base + jnp.arange(2, dtype=jnp.int32)
    return jnp.where((positions < split)[None, :, None], first_part, second_part)


def on_device(loaded, counts, short_taps, filters, skip_gain, out_weight):
    my_index = lax.axis_index("seq")
    block_rows = filters.shape[0]
    parity = my_index % 2
    mate_count = from_partner(counts, "seq", 0)
    first_count = jnp.where(parity == 0, counts[0], mate_count[0])
    send_start = block_rows * (1 - parity)
    half = lax.dynamic_slice_in_dim(loaded, send_start, block_rows, 1)
    recv = from_partner(half, "seq", 0)
    first = jnp.where(parity == 0, loaded[:, :block_rows], recv)
    zeros = jnp.zeros_like(recv)
    second_src = jnp.where(
        parity == 0,
        jnp.concatenate([zeros, zeros, recv], axis=1),
        jnp.concatenate([zeros, loaded], axis=1),
    )
    second = lax.dynamic_slice_in_dim(second_src, 2 * block_rows - first_count, block_rows, 1)
    rows = jnp.arange(block_rows, dtype=jnp.int32)
    use_first = rows < first_count - block_rows * parity
    packed = jnp.where(use_first[None, :, None], first, second)
    rim_rows = rim_of(loaded, counts[0], mate_count[0], first_count, parity, block_rows)
    extended = jnp.concatenate([rim_rows, packed], axis=1).astype(jnp.float32)
    filtered = sum(
        (
            short_taps[tap_index][:, None, :]
            * extended[:, 2 - tap_index : 2 - tap_index + block_rows]
            for tap_index in range(3)
        )
    )
    signal = filtered[0] * filtered[1]
    conv, blocks = channel_conv(signal, filters, weight_blocks(out_weight))
    gated = (filtered[2] * (conv + skip_gain[None, :] * signal)).astype(jnp.bfloat16)
    every = lax.all_gather(gated, "chan", axis=1, tiled=True)
    mixed = project(blocks, every)
    return mixed.astype(jnp.bfloat16)


def solution(mesh):
    placed = (
        P(None, "seq", "chan"),
        P("seq"),
        P(None, None, "chan"),
        P("seq", "chan"),
        P("chan"),
        P("chan", None),
    )
    return jax.shard_map(
        on_device, mesh=mesh, in_specs=placed, out_specs=P("chan", "seq"), check_vma=False
    )
```

```python
import functools
import math

import jax
import jax.numpy as jnp
from jax import lax
from jax.sharding import PartitionSpec as P


def from_partner(value, axis, distance):
    mask = 2**distance
    pairs = [(source, source ^ mask) for source in range(lax.axis_size(axis))]
    return lax.ppermute(value, axis, pairs)


def shifted(block, axis, distance):
    devices = range(lax.axis_size(axis))
    route = [(i - distance, i) for i in devices if i - distance in devices]
    return lax.ppermute(block, axis, route)


def phase_table(out_ids, in_ids, modulus):
    product = out_ids[:, None] * in_ids[None, :] % modulus
    angle = product.astype(jnp.float32) * (2.0 * math.pi / modulus)
    return (jnp.cos(angle), jnp.sin(angle))


def channel_conv(signal, filters, blocks):
    stacked = jnp.swapaxes(jnp.stack([signal, filters]).astype(jnp.bfloat16), 1, 2)
    whole = lax.all_to_all(stacked, "seq", split_axis=1, concat_axis=2, tiled=True)
    streams, narrow, seq_len = whole.shape
    size = 2 * seq_len
    outer = 256
    inner = size // outer
    rows = seq_len // inner
    grid = whole.astype(jnp.float32).reshape(streams, narrow, rows, inner)
    outer_ids = jnp.arange(outer, dtype=jnp.int32)
    inner_ids = jnp.arange(inner, dtype=jnp.int32)
    cos_out, sin_out = phase_table(outer_ids, outer_ids[:rows], outer)
    cos_tw, sin_tw = phase_table(outer_ids, inner_ids, size)
    cos_in, sin_in = phase_table(inner_ids, inner_ids, inner)
    dot = functools.partial(jnp.einsum, precision=lax.Precision.HIGH)
    part_re = dot("kn,scnm->sckm", cos_out, grid)
    part_im = -dot("kn,scnm->sckm", sin_out, grid)
    twist_re = part_re * cos_tw + part_im * sin_tw
    twist_im = part_im * cos_tw - part_re * sin_tw
    spec_re = dot("sckm,mq->sckq", twist_re, cos_in) + dot("sckm,mq->sckq", twist_im, sin_in)
    spec_im = dot("sckm,mq->sckq", twist_im, cos_in) - dot("sckm,mq->sckq", twist_re, sin_in)
    prod_re = spec_re[0] * spec_re[1] - spec_im[0] * spec_im[1]
    prod_im = spec_re[0] * spec_im[1] + spec_im[0] * spec_re[1]
    back_re = dot("ckq,qm->ckm", prod_re, cos_in) - dot("ckq,qm->ckm", prod_im, sin_in)
    back_im = dot("ckq,qm->ckm", prod_im, cos_in) + dot("ckq,qm->ckm", prod_re, sin_in)
    turn_re = back_re * cos_tw - back_im * sin_tw
    turn_im = back_im * cos_tw + back_re * sin_tw
    series = dot("kn,ckm->cnm", cos_out, turn_re) - dot("kn,ckm->cnm", sin_out, turn_im)
    series = (series.reshape(narrow, seq_len) * (1.0 / size)).astype(jnp.bfloat16)
    series, blocks = lax.optimization_barrier((series, blocks))
    back = lax.all_to_all(series, "seq", split_axis=1, concat_axis=0, tiled=True)
    return back.T.astype(jnp.float32), blocks


def weight_blocks(out_weight):
    count = lax.axis_size("chan")
    me = lax.axis_index("chan")
    width = out_weight.shape[1] // count
    blocks = [lax.dynamic_slice_in_dim(out_weight, me * width, width, 1)]
    for step in range(1, count):
        piece = lax.dynamic_slice_in_dim(out_weight, (me + step) % count * width, width, 1)
        pairs = [(source, (source + step) % count) for source in range(count)]
        blocks.append(lax.ppermute(piece, "chan", pairs))
    return blocks


def project(blocks, every):
    count = len(blocks)
    me = lax.axis_index("chan")
    order = (me - jnp.arange(count, dtype=jnp.int32)) % count
    columns = jnp.take(jnp.stack(blocks), order, axis=0)
    columns = columns.reshape(count * blocks[0].shape[0], blocks[0].shape[1])
    return lax.dot_general(
        columns, every, (((0,), (1,)), ((), ())), preferred_element_type=jnp.float32
    )


def on_device(loaded, counts, short_taps, filters, skip_gain, out_weight):
    my_index = lax.axis_index("seq")
    block_rows = filters.shape[0]
    parity = my_index % 2
    mate_count = loaded.shape[1] - counts[0]
    first_count = jnp.where(parity == 0, counts[0], mate_count)
    send_start = block_rows * (1 - parity)
    half = lax.dynamic_slice_in_dim(loaded, send_start, block_rows, 1)
    recv = from_partner(half, "seq", 0)
    first = jnp.where(parity == 0, loaded[:, :block_rows], recv)
    zeros = jnp.zeros_like(recv)
    second_src = jnp.where(
        parity == 0,
        jnp.concatenate([zeros, zeros, recv], axis=1),
        jnp.concatenate([zeros, loaded], axis=1),
    )
    second = lax.dynamic_slice_in_dim(second_src, 2 * block_rows - first_count, block_rows, 1)
    rows = jnp.arange(block_rows, dtype=jnp.int32)
    use_first = rows < first_count - block_rows * parity
    packed = jnp.where(use_first[None, :, None], first, second)
    rim_rows = shifted(packed[:, block_rows - 2 :], "seq", 1)
    extended = jnp.concatenate([rim_rows, packed], axis=1).astype(jnp.float32)
    filtered = sum(
        (
            short_taps[tap_index][:, None, :]
            * extended[:, 2 - tap_index : 2 - tap_index + block_rows]
            for tap_index in range(3)
        )
    )
    signal = filtered[0] * filtered[1]
    conv, blocks = channel_conv(signal, filters, weight_blocks(out_weight))
    gated = (filtered[2] * (conv + skip_gain[None, :] * signal)).astype(jnp.bfloat16)
    every = lax.all_gather(gated, "chan", axis=1, tiled=True)
    mixed = project(blocks, every)
    return mixed.astype(jnp.bfloat16)


def solution(mesh):
    placed = (
        P(None, "seq", "chan"),
        P("seq"),
        P(None, None, "chan"),
        P("seq", "chan"),
        P("chan"),
        P("chan", None),
    )
    return jax.shard_map(
        on_device, mesh=mesh, in_specs=placed, out_specs=P("chan", "seq"), check_vma=False
    )
```

```python
import functools
import math

import jax
import jax.numpy as jnp
from jax import lax
from jax.sharding import PartitionSpec as P


def from_partner(value, axis, distance):
    mask = 2**distance
    pairs = [(source, source ^ mask) for source in range(lax.axis_size(axis))]
    return lax.ppermute(value, axis, pairs)


def shifted(block, axis, distance):
    devices = range(lax.axis_size(axis))
    route = [(i - distance, i) for i in devices if i - distance in devices]
    return lax.ppermute(block, axis, route)


def phase_table(out_ids, in_ids, modulus):
    product = out_ids[:, None] * in_ids[None, :] % modulus
    angle = product.astype(jnp.float32) * (2.0 * math.pi / modulus)
    return (jnp.cos(angle), jnp.sin(angle))


def split_dot(table, exact):
    high = table.astype(jnp.bfloat16)
    low = (table - high.astype(jnp.float32)).astype(jnp.bfloat16)
    total = None
    for part in (high, low):
        term = jnp.einsum("kn,scnm->sckm", part, exact, preferred_element_type=jnp.float32)
        total = term if total is None else total + term
    return total


def channel_conv(signal, filters, blocks):
    stacked = jnp.swapaxes(jnp.stack([signal, filters]).astype(jnp.bfloat16), 1, 2)
    whole = lax.all_to_all(stacked, "seq", split_axis=1, concat_axis=2, tiled=True)
    streams, narrow, seq_len = whole.shape
    size = 2 * seq_len
    outer = 256
    inner = size // outer
    rows = seq_len // inner
    outer_ids = jnp.arange(outer, dtype=jnp.int32)
    inner_ids = jnp.arange(inner, dtype=jnp.int32)
    cos_out, sin_out = phase_table(outer_ids, outer_ids[:rows], outer)
    cos_tw, sin_tw = phase_table(outer_ids, inner_ids, size)
    cos_in, sin_in = phase_table(inner_ids, inner_ids, inner)
    dot = functools.partial(jnp.einsum, precision=lax.Precision.HIGH)
    exact = whole.reshape(streams, narrow, rows, inner)
    part_re = split_dot(cos_out, exact)
    part_im = -split_dot(sin_out, exact)
    twist_re = part_re * cos_tw + part_im * sin_tw
    twist_im = part_im * cos_tw - part_re * sin_tw
    spec_re = dot("sckm,mq->sckq", twist_re, cos_in) + dot("sckm,mq->sckq", twist_im, sin_in)
    spec_im = dot("sckm,mq->sckq", twist_im, cos_in) - dot("sckm,mq->sckq", twist_re, sin_in)
    prod_re = spec_re[0] * spec_re[1] - spec_im[0] * spec_im[1]
    prod_im = spec_re[0] * spec_im[1] + spec_im[0] * spec_re[1]
    back_re = dot("ckq,qm->ckm", prod_re, cos_in) - dot("ckq,qm->ckm", prod_im, sin_in)
    back_im = dot("ckq,qm->ckm", prod_im, cos_in) + dot("ckq,qm->ckm", prod_re, sin_in)
    turn_re = back_re * cos_tw - back_im * sin_tw
    turn_im = back_im * cos_tw + back_re * sin_tw
    series = dot("kn,ckm->cnm", cos_out, turn_re) - dot("kn,ckm->cnm", sin_out, turn_im)
    series = (series.reshape(narrow, seq_len) * (1.0 / size)).astype(jnp.bfloat16)
    series, blocks = lax.optimization_barrier((series, blocks))
    back = lax.all_to_all(series, "seq", split_axis=1, concat_axis=0, tiled=True)
    return back.T.astype(jnp.float32), blocks


def weight_blocks(out_weight):
    count = lax.axis_size("chan")
    me = lax.axis_index("chan")
    width = out_weight.shape[1] // count
    blocks = [lax.dynamic_slice_in_dim(out_weight, me * width, width, 1)]
    for step in range(1, count):
        piece = lax.dynamic_slice_in_dim(out_weight, (me + step) % count * width, width, 1)
        pairs = [(source, (source + step) % count) for source in range(count)]
        blocks.append(lax.ppermute(piece, "chan", pairs))
    return blocks


def project(blocks, every):
    count = len(blocks)
    me = lax.axis_index("chan")
    order = (me - jnp.arange(count, dtype=jnp.int32)) % count
    columns = jnp.take(jnp.stack(blocks), order, axis=0)
    columns = columns.reshape(count * blocks[0].shape[0], blocks[0].shape[1])
    return lax.dot_general(
        columns, every, (((0,), (1,)), ((), ())), preferred_element_type=jnp.float32
    )


def on_device(loaded, counts, short_taps, filters, skip_gain, out_weight):
    my_index = lax.axis_index("seq")
    block_rows = filters.shape[0]
    parity = my_index % 2
    mate_count = loaded.shape[1] - counts[0]
    first_count = jnp.where(parity == 0, counts[0], mate_count)
    send_start = block_rows * (1 - parity)
    half = lax.dynamic_slice_in_dim(loaded, send_start, block_rows, 1)
    recv = from_partner(half, "seq", 0)
    first = jnp.where(parity == 0, loaded[:, :block_rows], recv)
    zeros = jnp.zeros_like(recv)
    second_src = jnp.where(
        parity == 0,
        jnp.concatenate([zeros, zeros, recv], axis=1),
        jnp.concatenate([zeros, loaded], axis=1),
    )
    second = lax.dynamic_slice_in_dim(second_src, 2 * block_rows - first_count, block_rows, 1)
    rows = jnp.arange(block_rows, dtype=jnp.int32)
    use_first = rows < first_count - block_rows * parity
    packed = jnp.where(use_first[None, :, None], first, second)
    rim_rows = shifted(packed[:, block_rows - 2 :], "seq", 1)
    extended = jnp.concatenate([rim_rows, packed], axis=1).astype(jnp.float32)
    filtered = sum(
        (
            short_taps[tap_index][:, None, :]
            * extended[:, 2 - tap_index : 2 - tap_index + block_rows]
            for tap_index in range(3)
        )
    )
    signal = filtered[0] * filtered[1]
    conv, blocks = channel_conv(signal, filters, weight_blocks(out_weight))
    gated = (filtered[2] * (conv + skip_gain[None, :] * signal)).astype(jnp.bfloat16)
    every = lax.all_gather(gated, "chan", axis=1, tiled=True)
    mixed = project(blocks, every)
    return mixed.astype(jnp.bfloat16)


def solution(mesh):
    placed = (
        P(None, "seq", "chan"),
        P("seq"),
        P(None, None, "chan"),
        P("seq", "chan"),
        P("chan"),
        P("chan", None),
    )
    return jax.shard_map(
        on_device, mesh=mesh, in_specs=placed, out_specs=P("chan", "seq"), check_vma=False
    )
```

```python
import functools
import math

import jax
import jax.numpy as jnp
from jax import lax
from jax.sharding import PartitionSpec as P


def from_partner(value, axis, distance):
    mask = 2**distance
    pairs = [(source, source ^ mask) for source in range(lax.axis_size(axis))]
    return lax.ppermute(value, axis, pairs)


def shifted(block, axis, distance):
    devices = range(lax.axis_size(axis))
    route = [(i - distance, i) for i in devices if i - distance in devices]
    return lax.ppermute(block, axis, route)


def phase_table(out_ids, in_ids, modulus):
    product = out_ids[:, None] * in_ids[None, :] % modulus
    angle = product.astype(jnp.float32) * (2.0 * math.pi / modulus)
    return (jnp.cos(angle), jnp.sin(angle))


def split_dot(table, exact):
    rounded = lax.reduce_precision(table, exponent_bits=8, mantissa_bits=7)
    high = rounded.astype(jnp.bfloat16)
    low = (table - rounded).astype(jnp.bfloat16)
    total = None
    for part in (high, low):
        term = jnp.einsum("kn,scnm->sckm", part, exact, preferred_element_type=jnp.float32)
        total = term if total is None else total + term
    return total


def channel_conv(signal, filters, blocks):
    stacked = jnp.swapaxes(jnp.stack([signal, filters]).astype(jnp.bfloat16), 1, 2)
    whole = lax.all_to_all(stacked, "seq", split_axis=1, concat_axis=2, tiled=True)
    streams, narrow, seq_len = whole.shape
    size = 2 * seq_len
    outer = 256
    inner = size // outer
    rows = seq_len // inner
    outer_ids = jnp.arange(outer, dtype=jnp.int32)
    inner_ids = jnp.arange(inner, dtype=jnp.int32)
    cos_out, sin_out = phase_table(outer_ids, outer_ids[:rows], outer)
    cos_tw, sin_tw = phase_table(outer_ids, inner_ids, size)
    cos_in, sin_in = phase_table(inner_ids, inner_ids, inner)
    dot = functools.partial(jnp.einsum, precision=lax.Precision.HIGH)
    exact = whole.reshape(streams, narrow, rows, inner)
    part_re = split_dot(cos_out, exact)
    part_im = -split_dot(sin_out, exact)
    twist_re = part_re * cos_tw + part_im * sin_tw
    twist_im = part_im * cos_tw - part_re * sin_tw
    spec_re = dot("sckm,mq->sckq", twist_re, cos_in) + dot("sckm,mq->sckq", twist_im, sin_in)
    spec_im = dot("sckm,mq->sckq", twist_im, cos_in) - dot("sckm,mq->sckq", twist_re, sin_in)
    prod_re = spec_re[0] * spec_re[1] - spec_im[0] * spec_im[1]
    prod_im = spec_re[0] * spec_im[1] + spec_im[0] * spec_re[1]
    back_re = dot("ckq,qm->ckm", prod_re, cos_in) - dot("ckq,qm->ckm", prod_im, sin_in)
    back_im = dot("ckq,qm->ckm", prod_im, cos_in) + dot("ckq,qm->ckm", prod_re, sin_in)
    turn_re = back_re * cos_tw - back_im * sin_tw
    turn_im = back_im * cos_tw + back_re * sin_tw
    series = dot("kn,ckm->cnm", cos_out, turn_re) - dot("kn,ckm->cnm", sin_out, turn_im)
    series = (series.reshape(narrow, seq_len) * (1.0 / size)).astype(jnp.bfloat16)
    series, blocks = lax.optimization_barrier((series, blocks))
    back = lax.all_to_all(series, "seq", split_axis=1, concat_axis=0, tiled=True)
    return back.T.astype(jnp.float32), blocks


def weight_blocks(out_weight):
    count = lax.axis_size("chan")
    me = lax.axis_index("chan")
    width = out_weight.shape[1] // count
    blocks = [lax.dynamic_slice_in_dim(out_weight, me * width, width, 1)]
    for step in range(1, count):
        piece = lax.dynamic_slice_in_dim(out_weight, (me + step) % count * width, width, 1)
        pairs = [(source, (source + step) % count) for source in range(count)]
        blocks.append(lax.ppermute(piece, "chan", pairs))
    return blocks


def project(blocks, every):
    count = len(blocks)
    me = lax.axis_index("chan")
    order = (me - jnp.arange(count, dtype=jnp.int32)) % count
    columns = jnp.take(jnp.stack(blocks), order, axis=0)
    columns = columns.reshape(count * blocks[0].shape[0], blocks[0].shape[1])
    return lax.dot_general(
        columns, every, (((0,), (1,)), ((), ())), preferred_element_type=jnp.float32
    )


def on_device(loaded, counts, short_taps, filters, skip_gain, out_weight):
    my_index = lax.axis_index("seq")
    block_rows = filters.shape[0]
    parity = my_index % 2
    mate_count = loaded.shape[1] - counts[0]
    first_count = jnp.where(parity == 0, counts[0], mate_count)
    send_start = block_rows * (1 - parity)
    half = lax.dynamic_slice_in_dim(loaded, send_start, block_rows, 1)
    recv = from_partner(half, "seq", 0)
    first = jnp.where(parity == 0, loaded[:, :block_rows], recv)
    zeros = jnp.zeros_like(recv)
    second_src = jnp.where(
        parity == 0,
        jnp.concatenate([zeros, zeros, recv], axis=1),
        jnp.concatenate([zeros, loaded], axis=1),
    )
    second = lax.dynamic_slice_in_dim(second_src, 2 * block_rows - first_count, block_rows, 1)
    rows = jnp.arange(block_rows, dtype=jnp.int32)
    use_first = rows < first_count - block_rows * parity
    packed = jnp.where(use_first[None, :, None], first, second)
    rim_rows = shifted(packed[:, block_rows - 2 :], "seq", 1)
    extended = jnp.concatenate([rim_rows, packed], axis=1).astype(jnp.float32)
    filtered = sum(
        (
            short_taps[tap_index][:, None, :]
            * extended[:, 2 - tap_index : 2 - tap_index + block_rows]
            for tap_index in range(3)
        )
    )
    signal = filtered[0] * filtered[1]
    conv, blocks = channel_conv(signal, filters, weight_blocks(out_weight))
    gated = (filtered[2] * (conv + skip_gain[None, :] * signal)).astype(jnp.bfloat16)
    every = lax.all_gather(gated, "chan", axis=1, tiled=True)
    mixed = project(blocks, every)
    return mixed.astype(jnp.bfloat16)


def solution(mesh):
    placed = (
        P(None, "seq", "chan"),
        P("seq"),
        P(None, None, "chan"),
        P("seq", "chan"),
        P("chan"),
        P("chan", None),
    )
    return jax.shard_map(
        on_device, mesh=mesh, in_specs=placed, out_specs=P("chan", "seq"), check_vma=False
    )
```
